512 devices in a mesh: row: 16 (over z, core), col: 32 (over y, x).
Axes of the slice: x: 4, y: 8, z: 8, core: 2. Of those that a mesh axis runs over, the one named last changes fastest.
Arguments:
- a11: float32 [256, 256], replicated, may hold values from -1 to 400, as said below
- l11_bar: float32 [256, 256], replicated, may hold values from -24 to 24
- a21: float32 [32768, 256], P(('col', 'row')), may hold values from -72 to 72
- l21_bar: float32 [32768, 256], P(('col', 'row')), may hold values from -6 to 6
- s_bar: bfloat16 [32, 16, 64, 32768], P(None, 'row', None, 'col'), may hold values from -0.0625 to 0.0625
Outputs:
- a21_bar: float32 [32768, 256], P(('col', 'row'))
- a11_bar: float32 [256, 256], replicated
The draws below stay inside these ranges and needn't reach their ends.
Inputs may be any that keep to these rules, and one draw needn't show every extreme that they name: a11 is symmetric and each diagonal entry exceeds the sum of the magnitudes of the other entries of its row.
All inputs are finite; a program needn't handle non-finite values.
Results may differ from the reference program's by a relative error of at most 0.0036.
Values may be sent and summed in bfloat16 or wider, within the bound.
No kernel may reach another device: no remote copies, remote signals or barrier semaphores. Data moves between devices by JAX's collectives and lax.ppermute only.
A program may use at most 64 MiB of HBM per device.

```python
import jax
import jax.numpy as jnp
from jax import lax

PANEL = 256
PR = 64
M = 32768
N_ROW = 16
N_COL = 32


def draw_a11(key, part):
    first = jax.random.fold_in(key, 11)
    second = jax.random.fold_in(key, 12)
    spread = jax.random.uniform(first, (PANEL, PANEL), jnp.float32, -0.6, 0.6)
    spread = 0.5 * (spread + spread.T)
    spread = spread * (1.0 - jnp.eye(PANEL, dtype=jnp.float32))
    diagonal = jax.random.uniform(second, (PANEL,), jnp.float32, 200.0, 400.0)
    return spread + jnp.diag(diagonal)


def with_spikes(drawn, key, source, target, parts, factor):
    owner, partner = [(jnp.arange(drawn.shape[axis_at]) // (drawn.shape[axis_at] // parts)).reshape([-1 if axis == axis_at else 1 for axis in range(drawn.ndim)]) for axis_at in (source, target)]
    chosen = jax.random.permutation(key, parts)[partner]
    strong = (owner == chosen) | (owner == (partner + parts // 2) % parts)
    return jnp.where(strong, factor * drawn, drawn)


def block_scale(own_key, dims, shards, low, top_value):
    level, own = 1.0, jax.random.fold_in(own_key, 6)
    for dim, shards_of in shards:
        heights = jnp.exp(jax.random.uniform(jax.random.fold_in(own, dim), (shards_of,), jnp.float32, low / len(shards), top_value / len(shards)))
        level = level * jnp.repeat(heights, dims[dim] // shards_of).reshape([-1 if axis == dim else 1 for axis in range(len(dims))])
    return level


def gaussian(stream_key, dims, scale, limit, cuts=(), kind=jnp.bfloat16):
    array = scale * jax.random.normal(stream_key, dims, jnp.float32)
    if cuts:
        array = array * block_scale(stream_key, dims, cuts, -0.22, 0.18)
    return jnp.clip(array, -limit, limit).astype(kind)


def noise_with(key, shape, scale, most, split, heavy, held_as=jnp.bfloat16):
    array = scale * jax.random.normal(key, shape, jnp.float32)
    if split:
        array = array * block_scale(key, shape, split, -0.22, 0.18)
    return jnp.clip(with_spikes(array, jax.random.fold_in(key, 3), *heavy), -most, most).astype(held_as)


def setup_inputs(seed: int = 0) -> dict:
    key_list = jax.random.split(jax.random.key(seed), 6)
    return {
        "a11": draw_a11(jax.random.fold_in(key_list[5], 71), 0),
        "l11_bar": gaussian(key_list[1], (PANEL, PANEL), 4.0, 24.0, (), jnp.float32),
        "a21": gaussian(key_list[2], (M, PANEL), 12.0, 72.0, ((0, 512),), jnp.float32),
        "l21_bar": gaussian(key_list[3], (M, PANEL), 1.0, 6.0, ((0, 512),), jnp.float32),
        "s_bar": noise_with(key_list[4], (N_COL, N_ROW, PR, M), M ** -0.5, 0.0625, ((1, 16), (3, 32)), (3, 0, 32, 2.75)),
    }


def halve_lower(square):
    lower = jnp.tril(square)
    return lower - 0.5 * jnp.diag(jnp.diag(square))

def right_solve_t(factor, rhs):
    return lax.linalg.triangular_solve(factor, rhs, left_side=False, lower=True, transpose_a=True)

def right_solve(factor, rhs):
    return lax.linalg.triangular_solve(factor, rhs, left_side=False, lower=True, transpose_a=False)

def left_solve_t(factor, rhs):
    return lax.linalg.triangular_solve(factor, rhs, left_side=True, lower=True, transpose_a=True)

def reference(a11, l11_bar, a21, l21_bar, s_bar):
    highest = lax.Precision.HIGHEST
    l11 = jnp.linalg.cholesky(a11)
    l21 = right_solve_t(l11, a21)
    panel = l21.astype(jnp.bfloat16)
    width = panel.shape[1]
    blocks = s_bar.reshape(N_COL, N_ROW * PR, M)
    panel_blocks = panel.reshape(N_COL, N_ROW * PR, width)

    def visit(carry, inputs):
        block, panel_block = inputs
        forward = jnp.dot(block.astype(jnp.float32), panel.astype(jnp.float32), preferred_element_type=jnp.float32)
        carry = carry + lax.dot_general(block.astype(jnp.float32), panel_block.astype(jnp.float32), (((0,), (0,)), ((), ())), preferred_element_type=jnp.float32)
        return (carry, forward)
    start = jnp.zeros((M, width), jnp.float32)
    back_sum, forward_blocks = lax.scan(visit, start, (blocks, panel_blocks))
    trail = l21_bar - forward_blocks.reshape(M, width) - back_sum
    a21_bar = right_solve(l11, trail)
    coupling = jnp.dot(trail.T, panel.astype(jnp.float32), precision=highest)
    l11_total = l11_bar - left_solve_t(l11, coupling)
    middle = halve_lower(jnp.dot(l11.T, l11_total, precision=highest))
    left = left_solve_t(l11, middle)
    whole = right_solve(l11, left)
    a11_bar = 0.5 * (whole + whole.T)
    return (a21_bar, a11_bar)
```

```python
import jax
import jax.numpy as jnp
from jax import lax
from jax.sharding import PartitionSpec as P


def halve_lower(square):
    lower = jnp.tril(square)
    return lower - 0.5 * jnp.diag(jnp.diag(square))


def right_solve_t(factor, rhs):
    return lax.linalg.triangular_solve(factor, rhs, left_side=False, lower=True, transpose_a=True)


def right_solve(factor, rhs):
    return lax.linalg.triangular_solve(factor, rhs, left_side=False, lower=True, transpose_a=False)


def left_solve_t(factor, rhs):
    return lax.linalg.triangular_solve(factor, rhs, left_side=True, lower=True, transpose_a=True)


def inner_rows(left, right):
    return lax.dot_general(
        left, right, (((0,), (0,)), ((), ())), preferred_element_type=jnp.float32
    )


def gather_rows(part, axis, size):
    spread = jnp.broadcast_to(part[None], (size,) + part.shape)
    return lax.all_to_all(spread, axis, 0, 0, tiled=True).reshape(-1, part.shape[-1])


def scatter_sum(whole, axis, size):
    pieces = whole.reshape(size, -1, whole.shape[-1])
    return lax.all_to_all(pieces, axis, 0, 0, tiled=True).sum(0)


def all_sum(square, axes, size):
    flat = square.reshape(size, -1)
    mine = lax.all_to_all(flat, axes, 0, 0, tiled=True).sum(0, keepdims=True)
    whole = lax.all_to_all(jnp.broadcast_to(mine, flat.shape), axes, 0, 0, tiled=True)
    return whole.reshape(square.shape)


def body(a11, l11_bar, a21, l21_bar, s_bar):
    highest = lax.Precision.HIGHEST
    n_row = lax.axis_size("row")
    n_col = lax.axis_size("col")
    rows_own = a21.shape[0]
    blocks_here = s_bar.shape[0]
    tile = s_bar.reshape(blocks_here * rows_own, s_bar.shape[3])
    l11 = jnp.linalg.cholesky(a11)
    l21_own = right_solve_t(l11, a21)
    panel_own = l21_own.astype(jnp.bfloat16)
    panel_rows = gather_rows(panel_own, "col", n_col)
    panel_cols = lax.all_gather(panel_own, "row", axis=0, tiled=True)
    row_share = scatter_sum(
        jnp.dot(tile, panel_cols, preferred_element_type=jnp.float32), "col", n_col
    )
    col_share = scatter_sum(inner_rows(tile, panel_rows), "row", n_row)
    trail = l21_bar - row_share - col_share
    a21_bar = right_solve(l11, trail)
    panel_exact = panel_own.astype(jnp.float32)
    coupling = all_sum(
        jnp.dot(trail.T, panel_exact, precision=highest), ("row", "col"), n_row * n_col
    )
    l11_total = l11_bar - left_solve_t(l11, coupling)
    middle = halve_lower(jnp.dot(l11.T, l11_total, precision=highest))
    left = left_solve_t(l11, middle)
    whole = right_solve(l11, left)
    a11_bar = 0.5 * (whole + whole.T)
    return (a21_bar, a11_bar)


def solution(mesh):
    in_specs = (
        P(),
        P(),
        P(("col", "row"), None),
        P(("col", "row"), None),
        P(None, "row", None, "col"),
    )
    out_specs = (P(("col", "row"), None), P())
    return jax.shard_map(body, mesh=mesh, in_specs=in_specs, out_specs=out_specs, check_vma=False)
```

```python
import jax
import jax.numpy as jnp
from jax import lax
from jax.sharding import PartitionSpec as P


def halve_lower(square):
    lower = jnp.tril(square)
    return lower - 0.5 * jnp.diag(jnp.diag(square))


def right_solve_t(factor, rhs):
    return lax.linalg.triangular_solve(factor, rhs, left_side=False, lower=True, transpose_a=True)


def right_solve(factor, rhs):
    return lax.linalg.triangular_solve(factor, rhs, left_side=False, lower=True, transpose_a=False)


def left_solve_t(factor, rhs):
    return lax.linalg.triangular_solve(factor, rhs, left_side=True, lower=True, transpose_a=True)


def inner_rows(left, right, precision=None):
    return lax.dot_general(
        left, right, (((0,), (0,)), ((), ())), preferred_element_type=jnp.float32,
        precision=precision,
    )


def gather_rows(part, axis, size):
    spread = jnp.broadcast_to(part[None], (size,) + part.shape)
    return lax.all_to_all(spread, axis, 0, 0, tiled=True).reshape(-1, part.shape[-1])


def split_pair(values):
    high = values.astype(jnp.bfloat16)
    low = (values - high.astype(jnp.float32)).astype(jnp.bfloat16)
    return high, low


def body(a11, l11_bar, a21, l21_bar, s_bar):
    highest = lax.Precision.HIGHEST
    n_row = lax.axis_size("row")
    n_col = lax.axis_size("col")
    rows_own, width = a21.shape
    blocks_here = s_bar.shape[0]
    tile = s_bar.reshape(blocks_here * rows_own, s_bar.shape[3])
    l11 = jnp.linalg.cholesky(a11)
    l21_own = right_solve_t(l11, a21)
    panel_own = l21_own.astype(jnp.bfloat16)
    panel_rows = gather_rows(panel_own, "col", n_col)
    panel_cols = lax.all_gather(panel_own, "row", axis=0, tiled=True)
    forward = jnp.dot(tile, panel_cols, preferred_element_type=jnp.float32)
    backward = inner_rows(tile, panel_rows)
    panel_exact = panel_own.astype(jnp.float32)
    coupling_part = (
        inner_rows(l21_bar, panel_exact, highest)
        - inner_rows(forward, panel_rows.astype(jnp.float32), highest)
        - inner_rows(backward, panel_cols.astype(jnp.float32), highest)
    )
    high, low = split_pair(coupling_part)
    strip = width // n_col
    pieces = jnp.concatenate(
        [
            forward.astype(jnp.bfloat16).reshape(n_col, rows_own, width),
            high.reshape(n_col, strip, width),
            low.reshape(n_col, strip, width),
        ],
        axis=1,
    )
    got = lax.all_to_all(pieces, "col", 0, 0, tiled=True).astype(jnp.float32)
    row_share = got[:, :rows_own].sum(0)
    coupling_col = (got[:, rows_own:rows_own + strip] + got[:, rows_own + strip:]).sum(0)
    span = width // n_row
    spread = coupling_col.reshape(strip, n_row, span).transpose(1, 0, 2).reshape(n_row, strip * span)
    high, low = split_pair(spread)
    pieces = jnp.concatenate(
        [
            backward.astype(jnp.bfloat16).reshape(n_row, rows_own, width),
            jnp.concatenate([high, low], axis=1).reshape(n_row, 1, 2 * strip * span),
        ],
        axis=1,
    )
    got = lax.all_to_all(pieces, "row", 0, 0, tiled=True).astype(jnp.float32)
    col_share = got[:, :rows_own].sum(0)
    mine = (got[:, rows_own, : strip * span] + got[:, rows_own, strip * span:]).sum(0)
    n_all = n_row * n_col
    blocks = lax.all_to_all(
        jnp.broadcast_to(mine[None], (n_all, strip * span)), ("row", "col"), 0, 0, tiled=True
    )
    coupling = (
        blocks.reshape(n_row, n_col, strip, span).transpose(1, 2, 0, 3).reshape(width, width)
    )
    trail = l21_bar - row_share - col_share
    a21_bar = right_solve(l11, trail)
    l11_total = l11_bar - left_solve_t(l11, coupling)
    middle = halve_lower(jnp.dot(l11.T, l11_total, precision=highest))
    left = left_solve_t(l11, middle)
    whole = right_solve(l11, left)
    a11_bar = 0.5 * (whole + whole.T)
    return (a21_bar, a11_bar)


def solution(mesh):
    in_specs = (
        P(),
        P(),
        P(("col", "row"), None),
        P(("col", "row"), None),
        P(None, "row", None, "col"),
    )
    out_specs = (P(("col", "row"), None), P())
    return jax.shard_map(body, mesh=mesh, in_specs=in_specs, out_specs=out_specs, check_vma=False)
```

```python
import jax
import jax.numpy as jnp
from jax import lax
from jax.sharding import PartitionSpec as P


def halve_lower(square):
    lower = jnp.tril(square)
    return lower - 0.5 * jnp.diag(jnp.diag(square))


def right_solve_t(factor, rhs):
    return lax.linalg.triangular_solve(factor, rhs, left_side=False, lower=True, transpose_a=True)


def right_solve(factor, rhs):
    return lax.linalg.triangular_solve(factor, rhs, left_side=False, lower=True, transpose_a=False)


def left_solve_t(factor, rhs):
    return lax.linalg.triangular_solve(factor, rhs, left_side=True, lower=True, transpose_a=True)


def invert_lower(factor):
    eye = jnp.eye(factor.shape[0], dtype=factor.dtype)
    return lax.linalg.triangular_solve(factor, eye, left_side=True, lower=True)


def factor_and_invert(square):
    highest = lax.Precision.HIGHEST
    half = square.shape[0] // 2
    first = lax.linalg.cholesky(square[:half, :half], symmetrize_input=False)
    first_inv = invert_lower(first)
    below = jnp.dot(square[half:, :half], first_inv.T, precision=highest)
    rest = square[half:, half:] - jnp.dot(below, below.T, precision=highest)
    last = lax.linalg.cholesky(rest, symmetrize_input=False)
    last_inv = invert_lower(last)
    corner = -jnp.dot(jnp.dot(last_inv, below, precision=highest), first_inv, precision=highest)
    zeros = jnp.zeros((half, square.shape[0] - half), square.dtype)
    factor = jnp.block([[first, zeros], [below, last]])
    inverse = jnp.block([[first_inv, zeros], [corner, last_inv]])
    return factor, inverse


def inner_rows(left, right, precision=None):
    return lax.dot_general(
        left, right, (((0,), (0,)), ((), ())), preferred_element_type=jnp.float32,
        precision=precision,
    )


def gather_rows(part, axis, size):
    spread = jnp.broadcast_to(part[None], (size,) + part.shape)
    return lax.all_to_all(spread, axis, 0, 0, tiled=True).reshape(-1, part.shape[-1])


def split_pair(values):
    high = values.astype(jnp.bfloat16)
    low = (values - high.astype(jnp.float32)).astype(jnp.bfloat16)
    return high, low


def body(a11, l11_bar, a21, l21_bar, s_bar):
    highest = lax.Precision.HIGHEST
    n_row = lax.axis_size("row")
    n_col = lax.axis_size("col")
    rows_own, width = a21.shape
    blocks_here = s_bar.shape[0]
    tile = s_bar.reshape(blocks_here * rows_own, s_bar.shape[3])
    l11, inverse = factor_and_invert(a11)
    l21_own = jnp.dot(a21, inverse.T, precision=highest)
    panel_own = l21_own.astype(jnp.bfloat16)
    panel_rows = gather_rows(panel_own, "col", n_col)
    panel_cols = lax.all_gather(panel_own, "row", axis=0, tiled=True)
    forward = jnp.dot(tile, panel_cols, preferred_element_type=jnp.float32)
    backward = inner_rows(tile, panel_rows)
    panel_exact = panel_own.astype(jnp.float32)
    coupling_part = (
        inner_rows(l21_bar, panel_exact, highest)
        - inner_rows(forward, panel_rows.astype(jnp.float32), highest)
        - inner_rows(backward, panel_cols.astype(jnp.float32), highest)
    )
    high, low = split_pair(coupling_part)
    strip = width // n_col
    pieces = jnp.concatenate(
        [
            forward.astype(jnp.bfloat16).reshape(n_col, rows_own, width),
            high.reshape(n_col, strip, width),
            low.reshape(n_col, strip, width),
        ],
        axis=1,
    )
    got = lax.all_to_all(pieces, "col", 0, 0, tiled=True).astype(jnp.float32)
    row_share = got[:, :rows_own].sum(0)
    coupling_col = (got[:, rows_own:rows_own + strip] + got[:, rows_own + strip:]).sum(0)
    span = width // n_row
    spread = coupling_col.reshape(strip, n_row, span).transpose(1, 0, 2).reshape(n_row, strip * span)
    high, low = split_pair(spread)
    pieces = jnp.concatenate(
        [
            backward.astype(jnp.bfloat16).reshape(n_row, rows_own, width),
            jnp.concatenate([high, low], axis=1).reshape(n_row, 1, 2 * strip * span),
        ],
        axis=1,
    )
    got = lax.all_to_all(pieces, "row", 0, 0, tiled=True).astype(jnp.float32)
    col_share = got[:, :rows_own].sum(0)
    mine = (got[:, rows_own, : strip * span] + got[:, rows_own, strip * span:]).sum(0)
    n_all = n_row * n_col
    blocks = lax.all_to_all(
        jnp.broadcast_to(mine[None], (n_all, strip * span)), ("row", "col"), 0, 0, tiled=True
    )
    coupling = (
        blocks.reshape(n_row, n_col, strip, span).transpose(1, 2, 0, 3).reshape(width, width)
    )
    trail = l21_bar - row_share - col_share
    a21_bar = jnp.dot(trail, inverse, precision=highest)
    l11_total = l11_bar - jnp.dot(inverse.T, coupling, precision=highest)
    middle = halve_lower(jnp.dot(l11.T, l11_total, precision=highest))
    left = jnp.dot(inverse.T, middle, precision=highest)
    whole = jnp.dot(left, inverse, precision=highest)
    a11_bar = 0.5 * (whole + whole.T)
    return (a21_bar, a11_bar)


def solution(mesh):
    in_specs = (
        P(),
        P(),
        P(("col", "row"), None),
        P(("col", "row"), None),
        P(None, "row", None, "col"),
    )
    out_specs = (P(("col", "row"), None), P())
    return jax.shard_map(body, mesh=mesh, in_specs=in_specs, out_specs=out_specs, check_vma=False)
```

```python
import jax
import jax.numpy as jnp
from jax import lax
from jax.sharding import PartitionSpec as P


def halve_lower(square):
    row = lax.broadcasted_iota(jnp.int32, square.shape, 0)
    col = lax.broadcasted_iota(jnp.int32, square.shape, 1)
    return jnp.where(row > col, square, jnp.where(row == col, 0.5 * square, 0.0))


def right_solve_t(factor, rhs):
    return lax.linalg.triangular_solve(factor, rhs, left_side=False, lower=True, transpose_a=True)


def right_solve(factor, rhs):
    return lax.linalg.triangular_solve(factor, rhs, left_side=False, lower=True, transpose_a=False)


def left_solve_t(factor, rhs):
    return lax.linalg.triangular_solve(factor, rhs, left_side=True, lower=True, transpose_a=True)


def invert_lower(factor):
    eye = jnp.eye(factor.shape[0], dtype=factor.dtype)
    return lax.linalg.triangular_solve(factor, eye, left_side=True, lower=True)


def factor_and_invert(square):
    highest = lax.Precision.HIGHEST
    half = square.shape[0] // 2
    first = lax.linalg.cholesky(square[:half, :half], symmetrize_input=False)
    first_inv = invert_lower(first)
    below = jnp.dot(square[half:, :half], first_inv.T, precision=highest)
    rest = square[half:, half:] - jnp.dot(below, below.T, precision=highest)
    last = lax.linalg.cholesky(rest, symmetrize_input=False)
    last_inv = invert_lower(last)
    corner = -jnp.dot(jnp.dot(last_inv, below, precision=highest), first_inv, precision=highest)
    zeros = jnp.zeros((half, square.shape[0] - half), square.dtype)
    factor = jnp.block([[first, zeros], [below, last]])
    inverse = jnp.block([[first_inv, zeros], [corner, last_inv]])
    return factor, inverse


def inner_rows(left, right, precision=None):
    return lax.dot_general(
        left, right, (((0,), (0,)), ((), ())), preferred_element_type=jnp.float32,
        precision=precision,
    )


def gather_rows(part, axis, size):
    spread = jnp.broadcast_to(part[None], (size,) + part.shape)
    return lax.all_to_all(spread, axis, 0, 0, tiled=True).reshape(-1, part.shape[-1])


def split_pair(values):
    high = values.astype(jnp.bfloat16)
    low = (values - high.astype(jnp.float32)).astype(jnp.bfloat16)
    return high, low


def body(a11, l11_bar, a21, l21_bar, s_bar):
    highest = lax.Precision.HIGHEST
    n_row = lax.axis_size("row")
    n_col = lax.axis_size("col")
    rows_own, width = a21.shape
    blocks_here = s_bar.shape[0]
    tile = s_bar.reshape(blocks_here * rows_own, s_bar.shape[3])
    l11, inverse = factor_and_invert(a11)
    l21_own = jnp.dot(a21, inverse.T, precision=highest)
    panel_own = l21_own.astype(jnp.bfloat16)
    panel_rows = gather_rows(panel_own, "col", n_col)
    panel_cols = lax.all_gather(panel_own, "row", axis=0, tiled=True)
    forward = jnp.dot(tile, panel_cols, preferred_element_type=jnp.float32)
    backward = inner_rows(tile, panel_rows)
    panel_exact = panel_own.astype(jnp.float32)
    cross = inner_rows(panel_cols.astype(jnp.float32), backward, highest)
    coupling_part = inner_rows(l21_bar, panel_exact, highest) - cross - cross.T
    high, low = split_pair(coupling_part)
    strip = width // n_col
    pieces = jnp.concatenate(
        [
            forward.astype(jnp.bfloat16).reshape(n_col, rows_own, width),
            high.reshape(n_col, strip, width),
            low.reshape(n_col, strip, width),
        ],
        axis=1,
    )
    got = lax.all_to_all(pieces, "col", 0, 0, tiled=True)
    row_share = got[:, :rows_own].astype(jnp.float32).sum(0)
    coupling_col = (
        got[:, rows_own:rows_own + strip].astype(jnp.float32).sum(0)
        + got[:, rows_own + strip:].astype(jnp.float32).sum(0)
    )
    span = strip * width // n_row
    high, low = split_pair(coupling_col.reshape(n_row, span))
    pieces = jnp.concatenate(
        [
            backward.astype(jnp.bfloat16).reshape(n_row, rows_own, width),
            jnp.concatenate([high, low], axis=1).reshape(n_row, 1, 2 * span),
        ],
        axis=1,
    )
    got = lax.all_to_all(pieces, "row", 0, 0, tiled=True)
    col_share = got[:, :rows_own].astype(jnp.float32).sum(0)
    mine = (
        got[:, rows_own, :span].astype(jnp.float32).sum(0)
        + got[:, rows_own, span:].astype(jnp.float32).sum(0)
    )
    n_all = n_row * n_col
    coupling = lax.all_to_all(
        jnp.broadcast_to(mine[None], (n_all, span)), ("col", "row"), 0, 0, tiled=True
    ).reshape(width, width)
    trail = l21_bar - row_share - col_share
    a21_bar = jnp.dot(trail, inverse, precision=highest)
    l11_total = l11_bar - jnp.dot(inverse.T, coupling, precision=highest)
    middle = halve_lower(jnp.dot(l11.T, l11_total, precision=highest))
    left = jnp.dot(inverse.T, middle, precision=highest)
    whole = jnp.dot(left, inverse, precision=highest)
    a11_bar = 0.5 * (whole + whole.T)
    return (a21_bar, a11_bar)


def solution(mesh):
    in_specs = (
        P(),
        P(),
        P(("col", "row"), None),
        P(("col", "row"), None),
        P(None, "row", None, "col"),
    )
    out_specs = (P(("col", "row"), None), P())
    return jax.shard_map(body, mesh=mesh, in_specs=in_specs, out_specs=out_specs, check_vma=False)
```

```python
import jax
import jax.numpy as jnp
from jax import lax
from jax.sharding import PartitionSpec as P


def halve_lower(square):
    row = lax.broadcasted_iota(jnp.int32, square.shape, 0)
    col = lax.broadcasted_iota(jnp.int32, square.shape, 1)
    return jnp.where(row > col, square, jnp.where(row == col, 0.5 * square, 0.0))


def right_solve_t(factor, rhs):
    return lax.linalg.triangular_solve(factor, rhs, left_side=False, lower=True, transpose_a=True)


def right_solve(factor, rhs):
    return lax.linalg.triangular_solve(factor, rhs, left_side=False, lower=True, transpose_a=False)


def left_solve_t(factor, rhs):
    return lax.linalg.triangular_solve(factor, rhs, left_side=True, lower=True, transpose_a=True)


def invert_lower(factor):
    eye = jnp.eye(factor.shape[0], dtype=factor.dtype)
    return lax.linalg.triangular_solve(factor, eye, left_side=True, lower=True)


def factor_and_invert(square):
    highest = lax.Precision.HIGHEST
    half = square.shape[0] // 2
    first = lax.linalg.cholesky(square[:half, :half], symmetrize_input=False)
    first_inv = invert_lower(first)
    below = jnp.dot(square[half:, :half], first_inv.T, precision=highest)
    rest = square[half:, half:] - jnp.dot(below, below.T, precision=highest)
    last = lax.linalg.cholesky(rest, symmetrize_input=False)
    last_inv = invert_lower(last)
    corner = -jnp.dot(jnp.dot(last_inv, below, precision=highest), first_inv, precision=highest)
    zeros = jnp.zeros((half, square.shape[0] - half), square.dtype)
    factor = jnp.block([[first, zeros], [below, last]])
    inverse = jnp.block([[first_inv, zeros], [corner, last_inv]])
    return factor, inverse


def inner_rows(left, right, precision=None):
    return lax.dot_general(
        left, right, (((0,), (0,)), ((), ())), preferred_element_type=jnp.float32,
        precision=precision,
    )


def gather_rows(part, axis, size):
    spread = jnp.broadcast_to(part[None], (size,) + part.shape)
    return lax.all_to_all(spread, axis, 0, 0, tiled=True).reshape(-1, part.shape[-1])


def split_pair(values):
    high = values.astype(jnp.bfloat16)
    low = (values - high.astype(jnp.float32)).astype(jnp.bfloat16)
    return high, low


def body(a11, l11_bar, a21, l21_bar, s_bar):
    highest = lax.Precision.HIGHEST
    n_row = lax.axis_size("row")
    n_col = lax.axis_size("col")
    rows_own, width = a21.shape
    blocks_here = s_bar.shape[0]
    tile = s_bar.reshape(blocks_here * rows_own, s_bar.shape[3])
    a21_rows = gather_rows(a21, "col", n_col)
    l11, inverse = factor_and_invert(a11)
    l21_own = jnp.dot(a21, inverse.T, precision=highest)
    panel_own = l21_own.astype(jnp.bfloat16)
    panel_rows = jnp.dot(a21_rows, inverse.T, precision=highest).astype(jnp.bfloat16)
    panel_cols = lax.all_gather(panel_own, "row", axis=0, tiled=True)
    forward = jnp.dot(tile, panel_cols, preferred_element_type=jnp.float32)
    backward = inner_rows(tile, panel_rows)
    panel_exact = panel_own.astype(jnp.float32)
    cross = inner_rows(panel_cols.astype(jnp.float32), backward, highest)
    coupling_part = inner_rows(l21_bar, panel_exact, highest) - cross - cross.T
    high, low = split_pair(coupling_part)
    strip = width // n_col
    pieces = jnp.concatenate(
        [
            forward.astype(jnp.bfloat16).reshape(n_col, rows_own, width),
            high.reshape(n_col, strip, width),
            low.reshape(n_col, strip, width),
        ],
        axis=1,
    )
    got = lax.all_to_all(pieces, "col", 0, 0, tiled=True)
    row_share = got[:, :rows_own].astype(jnp.float32).sum(0)
    coupling_col = (
        got[:, rows_own:rows_own + strip].astype(jnp.float32).sum(0)
        + got[:, rows_own + strip:].astype(jnp.float32).sum(0)
    )
    span = strip * width // n_row
    high, low = split_pair(coupling_col.reshape(n_row, span))
    pieces = jnp.concatenate(
        [
            backward.astype(jnp.bfloat16).reshape(n_row, rows_own, width),
            jnp.concatenate([high, low], axis=1).reshape(n_row, 1, 2 * span),
        ],
        axis=1,
    )
    got = lax.all_to_all(pieces, "row", 0, 0, tiled=True)
    col_share = got[:, :rows_own].astype(jnp.float32).sum(0)
    mine = (
        got[:, rows_own, :span].astype(jnp.float32).sum(0)
        + got[:, rows_own, span:].astype(jnp.float32).sum(0)
    )
    n_all = n_row * n_col
    coupling = lax.all_to_all(
        jnp.broadcast_to(mine[None], (n_all, span)), ("col", "row"), 0, 0, tiled=True
    ).reshape(width, width)
    trail = l21_bar - row_share - col_share
    a21_bar = jnp.dot(trail, inverse, precision=highest)
    l11_total = l11_bar - jnp.dot(inverse.T, coupling, precision=highest)
    middle = halve_lower(jnp.dot(l11.T, l11_total, precision=highest))
    left = jnp.dot(inverse.T, middle, precision=highest)
    whole = jnp.dot(left, inverse, precision=highest)
    a11_bar = 0.5 * (whole + whole.T)
    return (a21_bar, a11_bar)


def solution(mesh):
    in_specs = (
        P(),
        P(),
        P(("col", "row"), None),
        P(("col", "row"), None),
        P(None, "row", None, "col"),
    )
    out_specs = (P(("col", "row"), None), P())
    return jax.shard_map(body, mesh=mesh, in_specs=in_specs, out_specs=out_specs, check_vma=False)
```

```python
import jax
import jax.numpy as jnp
from jax import lax
from jax.sharding import PartitionSpec as P


def halve_lower(square):
    row = lax.broadcasted_iota(jnp.int32, square.shape, 0)
    col = lax.broadcasted_iota(jnp.int32, square.shape, 1)
    return jnp.where(row > col, square, jnp.where(row == col, 0.5 * square, 0.0))


def right_solve_t(factor, rhs):
    return lax.linalg.triangular_solve(factor, rhs, left_side=False, lower=True, transpose_a=True)


def right_solve(factor, rhs):
    return lax.linalg.triangular_solve(factor, rhs, left_side=False, lower=True, transpose_a=False)


def left_solve_t(factor, rhs):
    return lax.linalg.triangular_solve(factor, rhs, left_side=True, lower=True, transpose_a=True)


def invert_lower(factor):
    eye = jnp.eye(factor.shape[0], dtype=factor.dtype)
    return lax.linalg.triangular_solve(factor, eye, left_side=True, lower=True)


def factor_and_invert(square):
    highest = lax.Precision.HIGHEST
    half = square.shape[0] // 2
    first = lax.linalg.cholesky(square[:half, :half], symmetrize_input=False)
    first_inv = invert_lower(first)
    below = jnp.dot(square[half:, :half], first_inv.T, precision=highest)
    rest = square[half:, half:] - jnp.dot(below, below.T, precision=highest)
    last = lax.linalg.cholesky(rest, symmetrize_input=False)
    last_inv = invert_lower(last)
    corner = -jnp.dot(jnp.dot(last_inv, below, precision=highest), first_inv, precision=highest)
    zeros = jnp.zeros((half, square.shape[0] - half), square.dtype)
    factor = jnp.block([[first, zeros], [below, last]])
    inverse = jnp.block([[first_inv, zeros], [corner, last_inv]])
    return factor, inverse


def inner_rows(left, right, precision=None):
    return lax.dot_general(
        left, right, (((0,), (0,)), ((), ())), preferred_element_type=jnp.float32,
        precision=precision,
    )


def gather_rows(part, axis, size):
    spread = jnp.broadcast_to(part[None], (size,) + part.shape)
    return lax.all_to_all(spread, axis, 0, 0, tiled=True).reshape(-1, part.shape[-1])


def split_pair(values):
    high = values.astype(jnp.bfloat16)
    low = (values - high.astype(jnp.float32)).astype(jnp.bfloat16)
    return high, low


def body(a11, l11_bar, a21, l21_bar, s_bar):
    highest = lax.Precision.HIGHEST
    n_row = lax.axis_size("row")
    n_col = lax.axis_size("col")
    rows_own, width = a21.shape
    blocks_here = s_bar.shape[0]
    tile = s_bar.reshape(blocks_here * rows_own, s_bar.shape[3])
    l11, inverse = factor_and_invert(a11)
    l21_own = jnp.dot(a21, inverse.T, precision=highest)
    panel_own = l21_own.astype(jnp.bfloat16)
    panel_rows = gather_rows(panel_own, "col", n_col)
    panel_cols = lax.all_gather(panel_own, "row", axis=0, tiled=True)
    forward = jnp.dot(tile, panel_cols, preferred_element_type=jnp.float32)
    backward = inner_rows(tile, panel_rows)
    panel_exact = panel_own.astype(jnp.float32)
    cross = inner_rows(panel_cols.astype(jnp.float32), backward, highest)
    coupling_part = inner_rows(l21_bar, panel_exact, highest) - cross - cross.T
    high, low = split_pair(coupling_part)
    strip = width // n_row
    pieces = jnp.concatenate(
        [
            backward.astype(jnp.bfloat16).reshape(n_row, rows_own, width),
            high.reshape(n_row, strip, width),
            low.reshape(n_row, strip, width),
        ],
        axis=1,
    )
    got = lax.all_to_all(pieces, "row", 0, 0, tiled=True)
    col_share = got[:, :rows_own].astype(jnp.float32).sum(0)
    coupling_row = (
        got[:, rows_own:rows_own + strip].astype(jnp.float32).sum(0)
        + got[:, rows_own + strip:].astype(jnp.float32).sum(0)
    )
    span = strip * width // n_col
    high, low = split_pair(coupling_row.reshape(n_col, span))
    pieces = jnp.concatenate(
        [
            forward.astype(jnp.bfloat16).reshape(n_col, rows_own, width),
            jnp.concatenate([high, low], axis=1).reshape(n_col, 1, 2 * span),
        ],
        axis=1,
    )
    got = lax.all_to_all(pieces, "col", 0, 0, tiled=True)
    row_share = got[:, :rows_own].astype(jnp.float32).sum(0)
    mine = (
        got[:, rows_own, :span].astype(jnp.float32).sum(0)
        + got[:, rows_own, span:].astype(jnp.float32).sum(0)
    )
    n_all = n_row * n_col
    coupling = lax.all_to_all(
        jnp.broadcast_to(mine[None], (n_all, span)), ("row", "col"), 0, 0, tiled=True
    ).reshape(width, width)
    trail = l21_bar - row_share - col_share
    a21_bar = jnp.dot(trail, inverse, precision=highest)
    l11_total = l11_bar - jnp.dot(inverse.T, coupling, precision=highest)
    middle = halve_lower(jnp.dot(l11.T, l11_total, precision=highest))
    left = jnp.dot(inverse.T, middle, precision=highest)
    whole = jnp.dot(left, inverse, precision=highest)
    a11_bar = 0.5 * (whole + whole.T)
    return (a21_bar, a11_bar)


def solution(mesh):
    in_specs = (
        P(),
        P(),
        P(("col", "row"), None),
        P(("col", "row"), None),
        P(None, "row", None, "col"),
    )
    out_specs = (P(("col", "row"), None), P())
    return jax.shard_map(body, mesh=mesh, in_specs=in_specs, out_specs=out_specs, check_vma=False)
```

```python
import jax
import jax.numpy as jnp
from jax import lax
from jax.sharding import PartitionSpec as P


def halve_lower(square):
    row = lax.broadcasted_iota(jnp.int32, square.shape, 0)
    col = lax.broadcasted_iota(jnp.int32, square.shape, 1)
    return jnp.where(row > col, square, jnp.where(row == col, 0.5 * square, 0.0))


def right_solve_t(factor, rhs):
    return lax.linalg.triangular_solve(factor, rhs, left_side=False, lower=True, transpose_a=True)


def right_solve(factor, rhs):
    return lax.linalg.triangular_solve(factor, rhs, left_side=False, lower=True, transpose_a=False)


def left_solve_t(factor, rhs):
    return lax.linalg.triangular_solve(factor, rhs, left_side=True, lower=True, transpose_a=True)


def invert_lower(factor):
    eye = jnp.eye(factor.shape[0], dtype=factor.dtype)
    return lax.linalg.triangular_solve(factor, eye, left_side=True, lower=True)


def factor_and_invert(square):
    highest = lax.Precision.HIGHEST
    half = square.shape[0] // 2
    first = lax.linalg.cholesky(square[:half, :half], symmetrize_input=False)
    first_inv = invert_lower(first)
    below = jnp.dot(square[half:, :half], first_inv.T, precision=highest)
    rest = square[half:, half:] - jnp.dot(below, below.T, precision=highest)
    last = lax.linalg.cholesky(rest, symmetrize_input=False)
    last_inv = invert_lower(last)
    corner = -jnp.dot(jnp.dot(last_inv, below, precision=highest), first_inv, precision=highest)
    zeros = jnp.zeros((half, square.shape[0] - half), square.dtype)
    factor = jnp.block([[first, zeros], [below, last]])
    inverse = jnp.block([[first_inv, zeros], [corner, last_inv]])
    return factor, inverse


def inner_rows(left, right, precision=None):
    return lax.dot_general(
        left, right, (((0,), (0,)), ((), ())), preferred_element_type=jnp.float32,
        precision=precision,
    )


def gather_rows(part, axis, size):
    spread = jnp.broadcast_to(part[None], (size,) + part.shape)
    return lax.all_to_all(spread, axis, 0, 0, tiled=True).reshape(-1, part.shape[-1])


def split_pair(values):
    high = values.astype(jnp.bfloat16)
    low = (values - high.astype(jnp.float32)).astype(jnp.bfloat16)
    return high, low


def body(a11, l11_bar, a21, l21_bar, s_bar):
    highest = lax.Precision.HIGHEST
    n_row = lax.axis_size("row")
    n_col = lax.axis_size("col")
    rows_own, width = a21.shape
    blocks_here = s_bar.shape[0]
    tile = s_bar.reshape(blocks_here * rows_own, s_bar.shape[3])
    l11, inverse = factor_and_invert(a11)
    l21_own = jnp.dot(a21, inverse.T, precision=highest)
    panel_own = l21_own.astype(jnp.bfloat16)
    panel_rows = gather_rows(panel_own, "col", n_col)
    panel_cols = lax.all_gather(panel_own, "row", axis=0, tiled=True)
    forward = jnp.dot(tile, panel_cols, preferred_element_type=jnp.float32)
    backward = inner_rows(tile, panel_rows)
    panel_exact = panel_own.astype(jnp.float32)
    cross = inner_rows(panel_cols.astype(jnp.float32), backward, highest)
    coupling_part = inner_rows(l21_bar, panel_exact, highest) - cross - cross.T
    high, low = split_pair(coupling_part)
    strip = width // n_col
    pieces = jnp.concatenate(
        [
            forward.astype(jnp.bfloat16).reshape(n_col, rows_own, width),
            high.reshape(n_col, strip, width),
            low.reshape(n_col, strip, width),
        ],
        axis=1,
    )
    got = lax.all_to_all(pieces, "col", 0, 0, tiled=True)
    row_share = got[:, :rows_own].astype(jnp.float32).sum(0)
    coupling_col = (
        got[:, rows_own:rows_own + strip].astype(jnp.float32).sum(0)
        + got[:, rows_own + strip:].astype(jnp.float32).sum(0)
    )
    got = lax.all_to_all(
        backward.astype(jnp.bfloat16).reshape(n_row, rows_own, width), "row", 0, 0, tiled=True
    )
    col_share = got.astype(jnp.float32).sum(0)
    coupling_rows = lax.all_gather(coupling_col, "row", axis=0, tiled=False).sum(0)
    coupling = lax.all_to_all(
        jnp.broadcast_to(coupling_rows[None], (n_col, strip, width)), "col", 0, 0, tiled=True
    ).reshape(width, width)
    trail = l21_bar - row_share - col_share
    a21_bar = jnp.dot(trail, inverse, precision=highest)
    l11_total = l11_bar - jnp.dot(inverse.T, coupling, precision=highest)
    middle = halve_lower(jnp.dot(l11.T, l11_total, precision=highest))
    left = jnp.dot(inverse.T, middle, precision=highest)
    whole = jnp.dot(left, inverse, precision=highest)
    a11_bar = 0.5 * (whole + whole.T)
    return (a21_bar, a11_bar)


def solution(mesh):
    in_specs = (
        P(),
        P(),
        P(("col", "row"), None),
        P(("col", "row"), None),
        P(None, "row", None, "col"),
    )
    out_specs = (P(("col", "row"), None), P())
    return jax.shard_map(body, mesh=mesh, in_specs=in_specs, out_specs=out_specs, check_vma=False)
```

```python
import jax
import jax.numpy as jnp
from jax import lax
from jax.sharding import PartitionSpec as P


def halve_lower(square):
    row = lax.broadcasted_iota(jnp.int32, square.shape, 0)
    col = lax.broadcasted_iota(jnp.int32, square.shape, 1)
    return jnp.where(row > col, square, jnp.where(row == col, 0.5 * square, 0.0))


def right_solve_t(factor, rhs):
    return lax.linalg.triangular_solve(factor, rhs, left_side=False, lower=True, transpose_a=True)


def right_solve(factor, rhs):
    return lax.linalg.triangular_solve(factor, rhs, left_side=False, lower=True, transpose_a=False)


def left_solve_t(factor, rhs):
    return lax.linalg.triangular_solve(factor, rhs, left_side=True, lower=True, transpose_a=True)


def invert_lower(factor):
    eye = jnp.eye(factor.shape[0], dtype=factor.dtype)
    return lax.linalg.triangular_solve(factor, eye, left_side=True, lower=True)


def factor_and_invert(square):
    highest = lax.Precision.HIGHEST
    half = square.shape[0] // 2
    first = lax.linalg.cholesky(square[:half, :half], symmetrize_input=False)
    first_inv = invert_lower(first)
    below = jnp.dot(square[half:, :half], first_inv.T, precision=highest)
    rest = square[half:, half:] - jnp.dot(below, below.T, precision=highest)
    last = lax.linalg.cholesky(rest, symmetrize_input=False)
    last_inv = invert_lower(last)
    corner = -jnp.dot(jnp.dot(last_inv, below, precision=highest), first_inv, precision=highest)
    zeros = jnp.zeros((half, square.shape[0] - half), square.dtype)
    factor = jnp.block([[first, zeros], [below, last]])
    inverse = jnp.block([[first_inv, zeros], [corner, last_inv]])
    return factor, inverse


def inner_rows(left, right, precision=None):
    return lax.dot_general(
        left, right, (((0,), (0,)), ((), ())), preferred_element_type=jnp.float32,
        precision=precision,
    )


def gather_rows(part, axis, size):
    spread = jnp.broadcast_to(part[None], (size,) + part.shape)
    return lax.all_to_all(spread, axis, 0, 0, tiled=True).reshape(-1, part.shape[-1])


def split_three(values):
    high = values.astype(jnp.bfloat16)
    rest = values - high.astype(jnp.float32)
    middle = rest.astype(jnp.bfloat16)
    low = (rest - middle.astype(jnp.float32)).astype(jnp.bfloat16)
    return high, middle, low


def body(a11, l11_bar, a21, l21_bar, s_bar):
    highest = lax.Precision.HIGHEST
    n_row = lax.axis_size("row")
    n_col = lax.axis_size("col")
    rows_own, width = a21.shape
    blocks_here = s_bar.shape[0]
    tile = s_bar.reshape(blocks_here * rows_own, s_bar.shape[3])
    l11, inverse = factor_and_invert(a11)
    l21_own = jnp.dot(a21, inverse.T, precision=highest)
    panel_own = l21_own.astype(jnp.bfloat16)
    panel_rows = gather_rows(panel_own, "col", n_col)
    panel_cols = lax.all_gather(panel_own, "row", axis=0, tiled=True)
    forward = jnp.dot(tile, panel_cols, preferred_element_type=jnp.float32)
    backward = inner_rows(tile, panel_rows)
    panel_exact = panel_own.astype(jnp.float32)
    cross = inner_rows(panel_cols.astype(jnp.float32), backward, highest)
    coupling_part = inner_rows(l21_bar, panel_exact, highest) - cross - cross.T
    parts = split_three(coupling_part)
    strip = width // n_col
    pieces = jnp.concatenate(
        [forward.astype(jnp.bfloat16).reshape(n_col, rows_own, width)]
        + [part.reshape(n_col, strip, width) for part in parts],
        axis=1,
    )
    got = lax.all_to_all(pieces, "col", 0, 0, tiled=True)
    row_share = got[:, :rows_own].astype(jnp.float32).sum(0)
    coupling_col = sum(
        got[:, rows_own + k * strip:rows_own + (k + 1) * strip].astype(jnp.float32).sum(0)
        for k in range(len(parts))
    )
    got = lax.all_to_all(
        backward.astype(jnp.bfloat16).reshape(n_row, rows_own, width), "row", 0, 0, tiled=True
    )
    col_share = got.astype(jnp.float32).sum(0)
    coupling_rows = lax.all_gather(coupling_col, "row", axis=0, tiled=False).sum(0)
    coupling = lax.all_to_all(
        jnp.broadcast_to(coupling_rows[None], (n_col, strip, width)), "col", 0, 0, tiled=True
    ).reshape(width, width)
    trail = l21_bar - row_share - col_share
    a21_bar = jnp.dot(trail, inverse, precision=highest)
    l11_total = l11_bar - jnp.dot(inverse.T, coupling, precision=highest)
    middle = halve_lower(jnp.dot(l11.T, l11_total, precision=highest))
    left = jnp.dot(inverse.T, middle, precision=highest)
    whole = jnp.dot(left, inverse, precision=highest)
    a11_bar = 0.5 * (whole + whole.T)
    return (a21_bar, a11_bar)


def solution(mesh):
    in_specs = (
        P(),
        P(),
        P(("col", "row"), None),
        P(("col", "row"), None),
        P(None, "row", None, "col"),
    )
    out_specs = (P(("col", "row"), None), P())
    return jax.shard_map(body, mesh=mesh, in_specs=in_specs, out_specs=out_specs, check_vma=False)
```

```python
import jax
import jax.numpy as jnp
from jax import lax
from jax.sharding import PartitionSpec as P


def halve_lower(square):
    row = lax.broadcasted_iota(jnp.int32, square.shape, 0)
    col = lax.broadcasted_iota(jnp.int32, square.shape, 1)
    return jnp.where(row > col, square, jnp.where(row == col, 0.5 * square, 0.0))


def right_solve_t(factor, rhs):
    return lax.linalg.triangular_solve(factor, rhs, left_side=False, lower=True, transpose_a=True)


def right_solve(factor, rhs):
    return lax.linalg.triangular_solve(factor, rhs, left_side=False, lower=True, transpose_a=False)


def left_solve_t(factor, rhs):
    return lax.linalg.triangular_solve(factor, rhs, left_side=True, lower=True, transpose_a=True)


def invert_lower(factor):
    eye = jnp.eye(factor.shape[0], dtype=factor.dtype)
    return lax.linalg.triangular_solve(factor, eye, left_side=True, lower=True)


def factor_and_invert(square):
    highest = lax.Precision.HIGHEST
    half = square.shape[0] // 2
    first = lax.linalg.cholesky(square[:half, :half], symmetrize_input=False)
    first_inv = invert_lower(first)
    below = jnp.dot(square[half:, :half], first_inv.T, precision=highest)
    rest = square[half:, half:] - jnp.dot(below, below.T, precision=highest)
    last = lax.linalg.cholesky(rest, symmetrize_input=False)
    last_inv = invert_lower(last)
    corner = -jnp.dot(jnp.dot(last_inv, below, precision=highest), first_inv, precision=highest)
    zeros = jnp.zeros((half, square.shape[0] - half), square.dtype)
    factor = jnp.block([[first, zeros], [below, last]])
    inverse = jnp.block([[first_inv, zeros], [corner, last_inv]])
    return factor, inverse


def inner_rows(left, right, precision=None):
    return lax.dot_general(
        left, right, (((0,), (0,)), ((), ())), preferred_element_type=jnp.float32,
        precision=precision,
    )


def gather_rows(part, axis, size):
    spread = jnp.broadcast_to(part[None], (size,) + part.shape)
    return lax.all_to_all(spread, axis, 0, 0, tiled=True).reshape(-1, part.shape[-1])


def split_pair(values):
    high = lax.reduce_precision(values, exponent_bits=8, mantissa_bits=7)
    low = values - high
    return high.astype(jnp.bfloat16), low.astype(jnp.bfloat16)


def body(a11, l11_bar, a21, l21_bar, s_bar):
    highest = lax.Precision.HIGHEST
    n_row = lax.axis_size("row")
    n_col = lax.axis_size("col")
    rows_own, width = a21.shape
    blocks_here = s_bar.shape[0]
    tile = s_bar.reshape(blocks_here * rows_own, s_bar.shape[3])
    l11, inverse = factor_and_invert(a11)
    l21_own = jnp.dot(a21, inverse.T, precision=highest)
    panel_own = l21_own.astype(jnp.bfloat16)
    panel_rows = gather_rows(panel_own, "col", n_col)
    panel_cols = lax.all_gather(panel_own, "row", axis=0, tiled=True)
    forward = jnp.dot(tile, panel_cols, preferred_element_type=jnp.float32)
    backward = inner_rows(tile, panel_rows)
    panel_exact = panel_own.astype(jnp.float32)
    cross = inner_rows(panel_cols.astype(jnp.float32), backward, highest)
    coupling_part = inner_rows(l21_bar, panel_exact, highest) - cross - cross.T
    high, low = split_pair(coupling_part)
    strip = width // n_col
    pieces = jnp.concatenate(
        [
            forward.astype(jnp.bfloat16).reshape(n_col, rows_own, width),
            high.reshape(n_col, strip, width),
            low.reshape(n_col, strip, width),
        ],
        axis=1,
    )
    got = lax.all_to_all(pieces, "col", 0, 0, tiled=True)
    row_share = got[:, :rows_own].astype(jnp.float32).sum(0)
    coupling_col = (
        got[:, rows_own:rows_own + strip].astype(jnp.float32).sum(0)
        + got[:, rows_own + strip:].astype(jnp.float32).sum(0)
    )
    got = lax.all_to_all(
        backward.astype(jnp.bfloat16).reshape(n_row, rows_own, width), "row", 0, 0, tiled=True
    )
    col_share = got.astype(jnp.float32).sum(0)
    coupling_rows = lax.all_gather(coupling_col, "row", axis=0, tiled=False).sum(0)
    coupling = lax.all_to_all(
        jnp.broadcast_to(coupling_rows[None], (n_col, strip, width)), "col", 0, 0, tiled=True
    ).reshape(width, width)
    trail = l21_bar - row_share - col_share
    a21_bar = jnp.dot(trail, inverse, precision=highest)
    l11_total = l11_bar - jnp.dot(inverse.T, coupling, precision=highest)
    middle = halve_lower(jnp.dot(l11.T, l11_total, precision=highest))
    left = jnp.dot(inverse.T, middle, precision=highest)
    whole = jnp.dot(left, inverse, precision=highest)
    a11_bar = 0.5 * (whole + whole.T)
    return (a21_bar, a11_bar)


def solution(mesh):
    in_specs = (
        P(),
        P(),
        P(("col", "row"), None),
        P(("col", "row"), None),
        P(None, "row", None, "col"),
    )
    out_specs = (P(("col", "row"), None), P())
    return jax.shard_map(body, mesh=mesh, in_specs=in_specs, out_specs=out_specs, check_vma=False)
```

```python
import jax
import jax.numpy as jnp
from jax import lax
from jax.experimental.layout import Layout, with_layout_constraint
from jax.sharding import PartitionSpec as P


def halve_lower(square):
    row = lax.broadcasted_iota(jnp.int32, square.shape, 0)
    col = lax.broadcasted_iota(jnp.int32, square.shape, 1)
    return jnp.where(row > col, square, jnp.where(row == col, 0.5 * square, 0.0))


def right_solve_t(factor, rhs):
    return lax.linalg.triangular_solve(factor, rhs, left_side=False, lower=True, transpose_a=True)


def right_solve(factor, rhs):
    return lax.linalg.triangular_solve(factor, rhs, left_side=False, lower=True, transpose_a=False)


def left_solve_t(factor, rhs):
    return lax.linalg.triangular_solve(factor, rhs, left_side=True, lower=True, transpose_a=True)


def invert_lower(factor):
    eye = jnp.eye(factor.shape[0], dtype=factor.dtype)
    return lax.linalg.triangular_solve(factor, eye, left_side=True, lower=True)


def factor_and_invert(square):
    highest = lax.Precision.HIGHEST
    half = square.shape[0] // 2
    first = lax.linalg.cholesky(square[:half, :half], symmetrize_input=False)
    first_inv = invert_lower(first)
    below = jnp.dot(square[half:, :half], first_inv.T, precision=highest)
    rest = square[half:, half:] - jnp.dot(below, below.T, precision=highest)
    last = lax.linalg.cholesky(rest, symmetrize_input=False)
    last_inv = invert_lower(last)
    corner = -jnp.dot(jnp.dot(last_inv, below, precision=highest), first_inv, precision=highest)
    zeros = jnp.zeros((half, square.shape[0] - half), square.dtype)
    factor = jnp.block([[first, zeros], [below, last]])
    inverse = jnp.block([[first_inv, zeros], [corner, last_inv]])
    return factor, inverse


def inner_rows(left, right, precision=None):
    return lax.dot_general(
        left, right, (((0,), (0,)), ((), ())), preferred_element_type=jnp.float32,
        precision=precision,
    )


def gather_rows(part, axis, size):
    spread = jnp.broadcast_to(part[None], (size,) + part.shape)
    return lax.all_to_all(spread, axis, 0, 0, tiled=True).reshape(-1, part.shape[-1])


def split_pair(values):
    high = lax.reduce_precision(values, exponent_bits=8, mantissa_bits=7)
    low = values - high
    return high.astype(jnp.bfloat16), low.astype(jnp.bfloat16)


def body(a11, l11_bar, a21, l21_bar, s_bar):
    highest = lax.Precision.HIGHEST
    n_row = lax.axis_size("row")
    n_col = lax.axis_size("col")
    rows_own, width = a21.shape
    blocks_here = s_bar.shape[0]
    tile = s_bar.reshape(blocks_here * rows_own, s_bar.shape[3])
    l11, inverse = factor_and_invert(a11)
    l21_own = jnp.dot(a21, inverse.T, precision=highest)
    panel_own = l21_own.astype(jnp.bfloat16)
    panel_rows = gather_rows(panel_own, "col", n_col)
    panel_cols = lax.all_gather(panel_own, "row", axis=0, tiled=True)
    forward = jnp.dot(tile, panel_cols, preferred_element_type=jnp.float32)
    backward = inner_rows(tile, panel_rows)
    panel_exact = panel_own.astype(jnp.float32)
    cross = inner_rows(panel_cols.astype(jnp.float32), backward, highest)
    coupling_part = inner_rows(l21_bar, panel_exact, highest) - cross - cross.T
    high, low = split_pair(coupling_part)
    strip = width // n_col
    pieces = jnp.concatenate(
        [
            with_layout_constraint(forward.astype(jnp.bfloat16), Layout((0, 1))).reshape(n_col, rows_own, width),
            high.reshape(n_col, strip, width),
            low.reshape(n_col, strip, width),
        ],
        axis=1,
    )
    got = lax.all_to_all(pieces, "col", 0, 0, tiled=True)
    row_share = got[:, :rows_own].astype(jnp.float32).sum(0)
    coupling_col = (
        got[:, rows_own:rows_own + strip].astype(jnp.float32).sum(0)
        + got[:, rows_own + strip:].astype(jnp.float32).sum(0)
    )
    got = lax.all_to_all(
        with_layout_constraint(backward.astype(jnp.bfloat16), Layout((0, 1))).reshape(n_row, rows_own, width),
        "row", 0, 0, tiled=True,
    )
    col_share = got.astype(jnp.float32).sum(0)
    coupling_rows = lax.all_gather(coupling_col, "row", axis=0, tiled=False).sum(0)
    coupling = lax.all_to_all(
        jnp.broadcast_to(coupling_rows[None], (n_col, strip, width)), "col", 0, 0, tiled=True
    ).reshape(width, width)
    trail = l21_bar - row_share - col_share
    a21_bar = jnp.dot(trail, inverse, precision=highest)
    l11_total = l11_bar - jnp.dot(inverse.T, coupling, precision=highest)
    middle = halve_lower(jnp.dot(l11.T, l11_total, precision=highest))
    left = jnp.dot(inverse.T, middle, precision=highest)
    whole = jnp.dot(left, inverse, precision=highest)
    a11_bar = 0.5 * (whole + whole.T)
    return (a21_bar, a11_bar)


def solution(mesh):
    in_specs = (
        P(),
        P(),
        P(("col", "row"), None),
        P(("col", "row"), None),
        P(None, "row", None, "col"),
    )
    out_specs = (P(("col", "row"), None), P())
    return jax.shard_map(body, mesh=mesh, in_specs=in_specs, out_specs=out_specs, check_vma=False)
```

```python
import jax
import jax.numpy as jnp
from jax import lax
from jax.experimental.layout import Layout, with_layout_constraint
from jax.sharding import PartitionSpec as P


def halve_lower(square):
    row = lax.broadcasted_iota(jnp.int32, square.shape, 0)
    col = lax.broadcasted_iota(jnp.int32, square.shape, 1)
    return jnp.where(row > col, square, jnp.where(row == col, 0.5 * square, 0.0))


def right_solve_t(factor, rhs):
    return lax.linalg.triangular_solve(factor, rhs, left_side=False, lower=True, transpose_a=True)


def right_solve(factor, rhs):
    return lax.linalg.triangular_solve(factor, rhs, left_side=False, lower=True, transpose_a=False)


def left_solve_t(factor, rhs):
    return lax.linalg.triangular_solve(factor, rhs, left_side=True, lower=True, transpose_a=True)


def invert_lower(factor):
    eye = jnp.eye(factor.shape[0], dtype=factor.dtype)
    return lax.linalg.triangular_solve(factor, eye, left_side=True, lower=True)


def factor_and_invert(square):
    highest = lax.Precision.HIGHEST
    half = square.shape[0] // 2
    first = lax.linalg.cholesky(square[:half, :half], symmetrize_input=False)
    first_inv = invert_lower(first)
    below = jnp.dot(square[half:, :half], first_inv.T, precision=highest)
    rest = square[half:, half:] - jnp.dot(below, below.T, precision=highest)
    last = lax.linalg.cholesky(rest, symmetrize_input=False)
    last_inv = invert_lower(last)
    corner = -jnp.dot(jnp.dot(last_inv, below, precision=highest), first_inv, precision=highest)
    zeros = jnp.zeros((half, square.shape[0] - half), square.dtype)
    factor = jnp.block([[first, zeros], [below, last]])
    inverse = jnp.block([[first_inv, zeros], [corner, last_inv]])
    return factor, inverse


def inner_rows(left, right, precision=None):
    return lax.dot_general(
        left, right, (((0,), (0,)), ((), ())), preferred_element_type=jnp.float32,
        precision=precision,
    )


def gather_rows(part, axis, size):
    spread = jnp.broadcast_to(part[None], (size,) + part.shape)
    return lax.all_to_all(spread, axis, 0, 0, tiled=True).reshape(-1, part.shape[-1])


def split_pair(values):
    high = lax.reduce_precision(values, exponent_bits=8, mantissa_bits=7)
    low = values - high
    return high.astype(jnp.bfloat16), low.astype(jnp.bfloat16)


def body(a11, l11_bar, a21, l21_bar, s_bar):
    highest = lax.Precision.HIGHEST
    n_row = lax.axis_size("row")
    n_col = lax.axis_size("col")
    rows_own, width = a21.shape
    blocks_here = s_bar.shape[0]
    tile = s_bar.reshape(blocks_here * rows_own, s_bar.shape[3])
    l11, inverse = factor_and_invert(a11)
    l21_own = jnp.dot(a21, inverse.T, precision=highest)
    panel_own = l21_own.astype(jnp.bfloat16)
    panel_rows = gather_rows(panel_own, "col", n_col)
    panel_cols = lax.all_gather(panel_own, "row", axis=0, tiled=True)
    forward = jnp.dot(tile, panel_cols, preferred_element_type=jnp.float32)
    backward = with_layout_constraint(inner_rows(tile, panel_rows), Layout((0, 1)))
    panel_exact = panel_own.astype(jnp.float32)
    cross = inner_rows(panel_cols.astype(jnp.float32), backward, highest)
    coupling_part = inner_rows(l21_bar, panel_exact, highest) - cross - cross.T
    high, low = split_pair(coupling_part)
    strip = width // n_col
    pieces = jnp.concatenate(
        [
            with_layout_constraint(forward.astype(jnp.bfloat16), Layout((0, 1))).reshape(n_col, rows_own, width),
            high.reshape(n_col, strip, width),
            low.reshape(n_col, strip, width),
        ],
        axis=1,
    )
    got = lax.all_to_all(pieces, "col", 0, 0, tiled=True)
    row_share = got[:, :rows_own].astype(jnp.float32).sum(0)
    coupling_col = (
        got[:, rows_own:rows_own + strip].astype(jnp.float32).sum(0)
        + got[:, rows_own + strip:].astype(jnp.float32).sum(0)
    )
    got = lax.all_to_all(
        with_layout_constraint(backward.astype(jnp.bfloat16), Layout((0, 1))).reshape(n_row, rows_own, width),
        "row", 0, 0, tiled=True,
    )
    col_share = got.astype(jnp.float32).sum(0)
    coupling_rows = lax.all_gather(coupling_col, "row", axis=0, tiled=False).sum(0)
    coupling = lax.all_to_all(
        jnp.broadcast_to(coupling_rows[None], (n_col, strip, width)), "col", 0, 0, tiled=True
    ).reshape(width, width)
    trail = l21_bar - row_share - col_share
    a21_bar = jnp.dot(trail, inverse, precision=highest)
    l11_total = l11_bar - jnp.dot(inverse.T, coupling, precision=highest)
    middle = halve_lower(jnp.dot(l11.T, l11_total, precision=highest))
    left = jnp.dot(inverse.T, middle, precision=highest)
    whole = jnp.dot(left, inverse, precision=highest)
    a11_bar = 0.5 * (whole + whole.T)
    return (a21_bar, a11_bar)


def solution(mesh):
    in_specs = (
        P(),
        P(),
        P(("col", "row"), None),
        P(("col", "row"), None),
        P(None, "row", None, "col"),
    )
    out_specs = (P(("col", "row"), None), P())
    return jax.shard_map(body, mesh=mesh, in_specs=in_specs, out_specs=out_specs, check_vma=False)
```

```python
import jax
import jax.numpy as jnp
from jax import lax
from jax.experimental.layout import Layout, with_layout_constraint
from jax.sharding import PartitionSpec as P


def halve_lower(square):
    row = lax.broadcasted_iota(jnp.int32, square.shape, 0)
    col = lax.broadcasted_iota(jnp.int32, square.shape, 1)
    return jnp.where(row > col, square, jnp.where(row == col, 0.5 * square, 0.0))


def right_solve_t(factor, rhs):
    return lax.linalg.triangular_solve(factor, rhs, left_side=False, lower=True, transpose_a=True)


def right_solve(factor, rhs):
    return lax.linalg.triangular_solve(factor, rhs, left_side=False, lower=True, transpose_a=False)


def left_solve_t(factor, rhs):
    return lax.linalg.triangular_solve(factor, rhs, left_side=True, lower=True, transpose_a=True)


def invert_lower(factor):
    eye = jnp.eye(factor.shape[0], dtype=factor.dtype)
    return lax.linalg.triangular_solve(factor, eye, left_side=True, lower=True)


def factor_and_invert(square):
    highest = lax.Precision.HIGHEST
    half = square.shape[0] // 2
    first = lax.linalg.cholesky(square[:half, :half], symmetrize_input=False)
    first_inv = with_layout_constraint(invert_lower(first), Layout((1, 0)))
    below = jnp.dot(square[half:, :half], first_inv.T, precision=highest)
    rest = square[half:, half:] - jnp.dot(below, below.T, precision=highest)
    last = lax.linalg.cholesky(rest, symmetrize_input=False)
    last_inv = with_layout_constraint(invert_lower(last), Layout((1, 0)))
    corner = -jnp.dot(jnp.dot(last_inv, below, precision=highest), first_inv, precision=highest)
    zeros = jnp.zeros((half, square.shape[0] - half), square.dtype)
    factor = jnp.block([[first, zeros], [below, last]])
    inverse = jnp.block([[first_inv, zeros], [corner, last_inv]])
    return factor, inverse


def inner_rows(left, right, precision=None):
    return lax.dot_general(
        left, right, (((0,), (0,)), ((), ())), preferred_element_type=jnp.float32,
        precision=precision,
    )


def gather_rows(part, axis, size):
    spread = jnp.broadcast_to(part[None], (size,) + part.shape)
    return lax.all_to_all(spread, axis, 0, 0, tiled=True).reshape(-1, part.shape[-1])


def split_pair(values):
    high = lax.reduce_precision(values, exponent_bits=8, mantissa_bits=7)
    low = values - high
    return high.astype(jnp.bfloat16), low.astype(jnp.bfloat16)


def body(a11, l11_bar, a21, l21_bar, s_bar):
    highest = lax.Precision.HIGHEST
    n_row = lax.axis_size("row")
    n_col = lax.axis_size("col")
    rows_own, width = a21.shape
    blocks_here = s_bar.shape[0]
    tile = s_bar.reshape(blocks_here * rows_own, s_bar.shape[3])
    l11, inverse = factor_and_invert(a11)
    l21_own = jnp.dot(a21, inverse.T, precision=highest)
    panel_own = l21_own.astype(jnp.bfloat16)
    panel_rows = gather_rows(panel_own, "col", n_col)
    panel_cols = lax.all_gather(panel_own, "row", axis=0, tiled=True)
    forward = jnp.dot(tile, panel_cols, preferred_element_type=jnp.float32)
    backward = with_layout_constraint(inner_rows(tile, panel_rows), Layout((0, 1)))
    panel_exact = panel_own.astype(jnp.float32)
    cross = inner_rows(panel_cols.astype(jnp.float32), backward, highest)
    coupling_part = inner_rows(l21_bar, panel_exact, highest) - cross - cross.T
    high, low = split_pair(coupling_part)
    strip = width // n_col
    pieces = jnp.concatenate(
        [
            with_layout_constraint(forward.astype(jnp.bfloat16), Layout((0, 1))).reshape(n_col, rows_own, width),
            high.reshape(n_col, strip, width),
            low.reshape(n_col, strip, width),
        ],
        axis=1,
    )
    got = lax.all_to_all(pieces, "col", 0, 0, tiled=True)
    row_share = got[:, :rows_own].astype(jnp.float32).sum(0)
    coupling_col = (
        got[:, rows_own:rows_own + strip].astype(jnp.float32).sum(0)
        + got[:, rows_own + strip:].astype(jnp.float32).sum(0)
    )
    got = lax.all_to_all(
        with_layout_constraint(backward.astype(jnp.bfloat16), Layout((0, 1))).reshape(n_row, rows_own, width),
        "row", 0, 0, tiled=True,
    )
    col_share = got.astype(jnp.float32).sum(0)
    coupling_rows = lax.all_gather(coupling_col, "row", axis=0, tiled=False).sum(0)
    coupling = lax.all_to_all(
        jnp.broadcast_to(coupling_rows[None], (n_col, strip, width)), "col", 0, 0, tiled=True
    ).reshape(width, width)
    trail = l21_bar - row_share - col_share
    a21_bar = jnp.dot(trail, inverse, precision=highest)
    l11_total = l11_bar - jnp.dot(inverse.T, coupling, precision=highest)
    middle = halve_lower(jnp.dot(l11.T, l11_total, precision=highest))
    left = jnp.dot(inverse.T, middle, precision=highest)
    whole = jnp.dot(left, inverse, precision=highest)
    a11_bar = 0.5 * (whole + whole.T)
    return (a21_bar, a11_bar)


def solution(mesh):
    in_specs = (
        P(),
        P(),
        P(("col", "row"), None),
        P(("col", "row"), None),
        P(None, "row", None, "col"),
    )
    out_specs = (P(("col", "row"), None), P())
    return jax.shard_map(body, mesh=mesh, in_specs=in_specs, out_specs=out_specs, check_vma=False)
```
